32 devices in a mesh: dp: 8 (over y, x, core), fsdp: 4 (over z).
Axes of the slice: x: 2, y: 2, z: 4, core: 2. Of those that a mesh axis runs over, the one named last changes fastest.
Arguments:
- activations: bfloat16 [8192, 4096], P(('dp', 'fsdp')), may hold values from -8 to 8
- cotangents: bfloat16 [8192, 4096], P('dp', 'fsdp'), may hold values from -8 to 8
- group_ids: int32 [32, 256], P(('dp', 'fsdp')), may hold values from 0 to 7, as said below
- weights: float32 [4096, 4096], P('fsdp', 'dp'), may hold values from -0.09375 to 0.09375
- first_moment: float32 [4096, 4096], P('fsdp', 'dp'), may hold values from -3 to 3
- second_moment: float32 [4096, 4096], P('fsdp', 'dp'), may hold values from 0.01 to 0.1
- fresh_noise: bfloat16 [4096, 4096], P('fsdp', 'dp'), may hold values from -6 to 6
- history: bfloat16 [16, 4096, 4096], P('dp', 'fsdp'), may hold values from -6 to 6
- slot_ids: int32 [16], P('dp'), may hold values from 0 to 15, each once
- band_coefs: float32 [16], replicated, may hold values from 0.3 to 1
- step_number: int32 [1], replicated, may hold values from 16 to 99999
- noise_mult: float32 [1], replicated, may hold values from 0.002 to 0.008
Outputs:
- new_weights: float32 [4096, 4096], P('fsdp', 'dp')
- new_first: float32 [4096, 4096], P('fsdp', 'dp')
- new_second: float32 [4096, 4096], P('fsdp', 'dp')
- noisy_mean: float32 [4096, 4096], P('fsdp', 'dp')
- gathered_weights: float32 [4096, 4096], P('fsdp')
- new_history: bfloat16 [16, 4096, 4096], P('dp', 'fsdp')
The draws below stay inside these ranges and needn't reach their ends.
Inputs may be any that keep to these rules, and one draw needn't show every extreme that they name: `group_ids`: in each row the ids never fall; each of the 8 ids names 1 to 64 tokens, one of them exactly 64. `slot_ids`: each cycle position is held by exactly one entry.
All inputs are finite; a program needn't handle non-finite values.
Results may differ from the reference program's by a relative error of at most 0.002.
Values may be sent and summed in bfloat16 or wider, within the bound.
No kernel may reach another device: no remote copies, remote signals or barrier semaphores. Data moves between devices by JAX's collectives and lax.ppermute only.
A program may use at most 192 MiB of HBM per device.

```python
import math
import jax
import jax.numpy as jnp
from jax import lax

D_IN = 4096
D_OUT = 4096
BAND = 16
GROUP_MOST = 64
TOK_DEV = 256
EX_DEV = 8
TOKENS = 8192
EXAMPLES = 256
N_DP = 8
N_FSDP = 4


def group_layout(key):
    row_count = N_DP * N_FSDP
    windows = TOK_DEV // GROUP_MOST
    base = jax.random.fold_in(key, 1201)
    key_single, key_offset, key_first, key_second = jax.random.split(base, 4)
    single = jax.random.randint(key_single, (row_count, 1), 0, windows)
    triple = (single + jax.random.randint(key_offset, (row_count, 1), 1, windows)) % windows
    first_cut = jax.random.randint(key_first, (row_count, windows), 1, GROUP_MOST)
    second_cut = (first_cut - 1 + jax.random.randint(key_second, (row_count, windows), 1, GROUP_MOST - 1)) % (GROUP_MOST - 1) + 1
    positions = jnp.arange(TOK_DEV, dtype=jnp.int32)
    window_of = positions // GROUP_MOST
    within = positions % GROUP_MOST
    first_at = jnp.take(first_cut, window_of, axis=1)
    second_at = jnp.take(second_cut, window_of, axis=1)
    starts = ((within == 0) & (window_of > 0))[None, :]
    inner_first = (within[None, :] == first_at) & (window_of[None, :] != single)
    inner_second = (within[None, :] == second_at) & (window_of[None, :] == triple)
    cuts = starts | inner_first | inner_second
    return jnp.cumsum(cuts.astype(jnp.int32), axis=1).astype(jnp.int32)


def shared_rows(key, labels, width, salt):
    row_count = N_DP * N_FSDP
    key_shared, key_amp, key_noise = jax.random.split(jax.random.fold_in(key, salt), 3)
    shared = jax.random.normal(key_shared, (row_count, EX_DEV, width), jnp.float32)
    amplitude = jax.random.uniform(key_amp, (row_count, TOK_DEV, 1), jnp.float32, 0.5, 1.5)
    noise = jax.random.normal(key_noise, (row_count, TOK_DEV, width), jnp.float32)
    per_token = jnp.take_along_axis(shared, labels[:, :, None], axis=1)
    values = jnp.clip(amplitude * per_token + noise, -8.0, 8.0)
    return values.reshape(row_count * TOK_DEV, width)


def draw_group_ids(key, part):
    return group_layout(key)


def draw_activations(key, part):
    return shared_rows(key, group_layout(key), D_IN, 31).astype(jnp.bfloat16)


def draw_cotangents(key, part):
    return shared_rows(key, group_layout(key), D_OUT, 57).astype(jnp.bfloat16)


def steps_of(rng, dims, pieces, low, largest):
    level, own = 1.0, jax.random.fold_in(rng, 6)
    for axis_at, blocks in pieces:
        heights = jnp.exp(jax.random.uniform(jax.random.fold_in(own, axis_at), (blocks,), jnp.float32, low / len(pieces), largest / len(pieces)))
        level = level * jnp.repeat(heights, dims[axis_at] // blocks).reshape([-1 if axis == axis_at else 1 for axis in range(len(dims))])
    return level


def gaussian(key, extent, scale, bound, cuts=(), kind=jnp.bfloat16):
    level = steps_of(key, extent, cuts, -0.22, 0.18) if cuts else 1.0
    result = jax.random.normal(key, extent, jnp.float32) * scale * level
    return jnp.minimum(jnp.maximum(result, -bound), bound).astype(kind)


def setup_inputs(seed: int = 0) -> dict:
    keys = jax.random.split(jax.random.key(seed), 13)
    return {
        "activations": draw_activations(jax.random.fold_in(keys[12], 71), 0),
        "cotangents": draw_cotangents(jax.random.fold_in(keys[12], 71), 0),
        "group_ids": draw_group_ids(jax.random.fold_in(keys[12], 71), 0),
        "weights": gaussian(keys[3], (D_OUT, D_IN), D_IN ** -0.5, 0.09375, ((0, 4), (1, 8)), jnp.float32),
        "first_moment": gaussian(keys[4], (D_OUT, D_IN), 0.2, 3.0, ((0, 4), (1, 8)), jnp.float32),
        "second_moment": jnp.clip(jnp.exp(math.log(0.1) - 2.3025851 * jax.random.uniform(keys[5], (D_OUT, D_IN), jnp.float32) ** steps_of(keys[5], (D_OUT, D_IN), ((0, 4), (1, 8)), -0.2, 0.2)), 0.01, 0.1),
        "fresh_noise": gaussian(keys[6], (D_OUT, D_IN), 1.0, 6.0, ((0, 4), (1, 8))),
        "history": gaussian(keys[7], (BAND, D_OUT, D_IN), 1.0, 6.0, ((0, 8), (1, 4))),
        "slot_ids": jax.random.permutation(keys[8], BAND).astype(jnp.int32),
        "band_coefs": jnp.clip(jax.random.uniform(keys[9], (BAND,), jnp.float32, 0.3, 1.0), 0.3, 1.0),
        "step_number": jax.random.randint(keys[10], (1,), BAND, 100000).astype(jnp.int32),
        "noise_mult": jnp.clip(jnp.exp(jax.random.uniform(keys[11], (1,), jnp.float32, math.log(0.002), math.log(0.008))), 0.002, 0.008),
    }


def clip_bound():
    return ((GROUP_MOST * GROUP_MOST / 4.0 + GROUP_MOST) * D_IN * D_OUT) ** 0.5

def reference(activations, cotangents, group_ids, weights, first_moment, second_moment, fresh_noise, history, slot_ids, band_coefs, step_number, noise_mult):
    clip = clip_bound()
    blocks = TOKENS // TOK_DEV
    input_rows = activations.reshape(blocks, TOK_DEV, D_IN).astype(jnp.float32)
    cotan_rows = cotangents.reshape(blocks, TOK_DEV, D_OUT).astype(jnp.float32)
    input_gram = jnp.einsum('bti,bsi->bts', input_rows, input_rows)
    cotan_gram = jnp.einsum('bti,bsi->bts', cotan_rows, cotan_rows)
    same = group_ids[:, :, None] == group_ids[:, None, :]
    row_terms = lax.optimization_barrier(jnp.sum(jnp.where(same, input_gram * cotan_gram, 0.0), axis=2))
    squared = lax.optimization_barrier(jnp.sum(jnp.where(same, row_terms[:, None, :], 0.0), axis=2))
    factor = clip / jnp.maximum(jnp.sqrt(squared), clip)
    scaled = (input_rows * factor[:, :, None]).astype(jnp.bfloat16).reshape(TOKENS, D_IN)
    gradient = jnp.dot(cotangents.T, scaled, preferred_element_type=jnp.float32)
    step_value = step_number[0]
    target = step_value % BAND
    lags = (step_value - slot_ids - 1) % BAND + 1
    columns = jnp.arange(BAND, dtype=jnp.int32)
    lag_weight = lax.optimization_barrier(jnp.sum(jnp.where(columns[None, :] == lags[:, None], band_coefs[None, :], 0.0), axis=1))
    banded = band_coefs[0] * fresh_noise.astype(jnp.float32)
    for position in range(BAND):
        banded = banded + lag_weight[position] * history[position].astype(jnp.float32)
    noisy_mean = (gradient + noise_mult[0] * clip * banded) / EXAMPLES
    new_first = 0.9 * first_moment + 0.1 * noisy_mean
    new_second = 0.999 * second_moment + 0.001 * noisy_mean * noisy_mean
    step_float = step_value.astype(jnp.float32)
    corrected_first = new_first / (1.0 - jnp.power(jnp.float32(0.9), step_float))
    corrected_second = new_second / (1.0 - jnp.power(jnp.float32(0.999), step_float))
    new_weights = weights - 0.002 * corrected_first / (jnp.sqrt(corrected_second) + 1e-08)
    gathered_weights = new_weights
    new_history = jnp.where((slot_ids == target)[:, None, None], fresh_noise[None], history)
    return (new_weights, new_first, new_second, noisy_mean, gathered_weights, new_history)
```

```python
import jax
import jax.numpy as jnp
from jax import lax
from jax.sharding import PartitionSpec as P

D_IN = 4096
D_OUT = 4096
BAND = 16
GROUP_MOST = 64
EX_DEV = 8


def clip_bound():
    return ((GROUP_MOST * GROUP_MOST / 4.0 + GROUP_MOST) * D_IN * D_OUT) ** 0.5


def make_body(n_dp, n_fsdp, chunks):
    def body(
        activations,
        cotangents,
        group_ids,
        weights,
        first_moment,
        second_moment,
        fresh_noise,
        history,
        slot_ids,
        band_coefs,
        step_number,
        noise_mult,
    ):
        clip = clip_bound()
        tok = activations.shape[0]
        d_in = activations.shape[1]
        out_local = cotangents.shape[1]
        cols = d_in // n_dp
        width = cols // chunks
        me = lax.axis_index("fsdp")
        step_value = step_number[0]
        target = step_value % BAND

        blocks = cotangents.reshape(n_fsdp, tok, out_local)
        partial_gram = jnp.einsum("ati,asi->ats", blocks, blocks, preferred_element_type=jnp.float32)
        cotan_gram = lax.psum_scatter(partial_gram, "fsdp", scatter_dimension=0, tiled=True)[0]
        input_gram = lax.dot_general(
            activations, activations, (((1,), (1,)), ((), ())), preferred_element_type=jnp.float32
        )
        labels = group_ids[0]
        same = labels[:, None] == labels[None, :]
        row_terms = jnp.sum(jnp.where(same, input_gram * cotan_gram, 0.0), axis=1)
        squared = jnp.sum(jnp.where(same, row_terms[None, :], 0.0), axis=1)
        factor = clip / jnp.maximum(jnp.sqrt(squared), clip)
        factors = lax.all_gather(factor, "fsdp", axis=0, tiled=False)

        lags = (step_value - slot_ids - 1) % BAND + 1
        columns = jnp.arange(BAND, dtype=jnp.int32)
        lag_weight = jnp.sum(
            jnp.where(columns[None, :] == lags[:, None], band_coefs[None, :], 0.0), axis=1
        )
        noise_scale = noise_mult[0] * clip

        act4 = activations.reshape(tok, n_dp, chunks, width)
        hist5 = history.reshape(history.shape[0], out_local, n_dp, chunks, width)

        def partial(block, src):
            src = jnp.clip(src, 0, n_fsdp - 1)
            fac = lax.dynamic_index_in_dim(factors, src, axis=0, keepdims=False)
            scaled = (block.astype(jnp.float32) * fac[:, None, None]).astype(jnp.bfloat16)
            cot = lax.dynamic_slice_in_dim(cotangents, src * tok, tok, axis=0)
            return jnp.einsum("to,tdw->dow", cot, scaled, preferred_element_type=jnp.float32)

        reduced = []
        for c in range(chunks):
            own = act4[:, :, c, :]
            acc = partial(own, me)
            right_msg = own
            left_msg = own
            for k in range(1, n_fsdp):
                right_msg = lax.ppermute(
                    right_msg, "fsdp", [(f, f + 1) for f in range(k - 1, n_fsdp - 1)]
                )
                left_msg = lax.ppermute(
                    left_msg, "fsdp", [(f, f - 1) for f in range(1, n_fsdp - k + 1)]
                )
                acc = acc + partial(right_msg, me - k) + partial(left_msg, me + k)
            hist_c = hist5[:, :, :, c, :]
            history_part = jnp.zeros(hist_c.shape[1:], jnp.float32)
            for position in range(hist_c.shape[0]):
                history_part = history_part + lag_weight[position] * hist_c[position].astype(jnp.float32)
            payload = acc + noise_scale * jnp.transpose(history_part, (1, 0, 2))
            reduced.append(lax.psum_scatter(payload, "dp", scatter_dimension=0, tiled=True)[0])
        combined = jnp.concatenate(reduced, axis=1)

        full_fresh = lax.all_gather(fresh_noise, "dp", axis=1, tiled=True)
        new_history = jnp.where((slot_ids == target)[:, None, None], full_fresh[None], history)

        examples = EX_DEV * n_dp * n_fsdp
        noisy_mean = (
            combined + noise_scale * band_coefs[0] * fresh_noise.astype(jnp.float32)
        ) / examples
        new_first = 0.9 * first_moment + 0.1 * noisy_mean
        new_second = 0.999 * second_moment + 0.001 * noisy_mean * noisy_mean
        step_float = step_value.astype(jnp.float32)
        corrected_first = new_first / (1.0 - jnp.power(jnp.float32(0.9), step_float))
        corrected_second = new_second / (1.0 - jnp.power(jnp.float32(0.999), step_float))
        new_weights = weights - 0.002 * corrected_first / (jnp.sqrt(corrected_second) + 1e-08)
        gathered_weights = lax.all_gather(new_weights, "dp", axis=1, tiled=True)
        return (new_weights, new_first, new_second, noisy_mean, gathered_weights, new_history)

    return body


def solution(mesh):
    n_dp = mesh.shape["dp"]
    n_fsdp = mesh.shape["fsdp"]
    cols = D_IN // n_dp
    chunks = max(1, min(4, cols // 128))
    in_specs = (
        P(("dp", "fsdp"), None),
        P("dp", "fsdp"),
        P(("dp", "fsdp"), None),
        P("fsdp", "dp"),
        P("fsdp", "dp"),
        P("fsdp", "dp"),
        P("fsdp", "dp"),
        P("dp", "fsdp", None),
        P("dp"),
        P(),
        P(),
        P(),
    )
    out_specs = (
        P("fsdp", "dp"),
        P("fsdp", "dp"),
        P("fsdp", "dp"),
        P("fsdp", "dp"),
        P("fsdp", None),
        P("dp", "fsdp", None),
    )
    return jax.shard_map(
        make_body(n_dp, n_fsdp, chunks),
        mesh=mesh,
        in_specs=in_specs,
        out_specs=out_specs,
        check_vma=False,
    )
```

```python
import jax
import jax.numpy as jnp
from jax import lax
from jax.sharding import PartitionSpec as P

D_IN = 4096
D_OUT = 4096
BAND = 16
GROUP_MOST = 64
EX_DEV = 8


def clip_bound():
    return ((GROUP_MOST * GROUP_MOST / 4.0 + GROUP_MOST) * D_IN * D_OUT) ** 0.5


def make_body(n_dp, n_fsdp):
    def body(
        activations,
        cotangents,
        group_ids,
        weights,
        first_moment,
        second_moment,
        fresh_noise,
        history,
        slot_ids,
        band_coefs,
        step_number,
        noise_mult,
    ):
        clip = clip_bound()
        tok = activations.shape[0]
        out_local = cotangents.shape[1]
        step_value = step_number[0]
        target = step_value % BAND

        full_act = lax.all_gather(activations, "fsdp", axis=0, tiled=True)

        blocks = cotangents.reshape(n_fsdp, tok, out_local)
        partial_gram = jnp.einsum("ati,asi->ats", blocks, blocks, preferred_element_type=jnp.float32)
        received = lax.all_to_all(partial_gram, "fsdp", 0, 0, tiled=True)
        cotan_gram = received[0]
        for part in range(1, n_fsdp):
            cotan_gram = cotan_gram + received[part]
        input_gram = lax.dot_general(
            activations, activations, (((1,), (1,)), ((), ())), preferred_element_type=jnp.float32
        )
        labels = group_ids[0]
        same = labels[:, None] == labels[None, :]
        row_terms = jnp.sum(jnp.where(same, input_gram * cotan_gram, 0.0), axis=1)
        squared = jnp.sum(jnp.where(same, row_terms[None, :], 0.0), axis=1)
        factor = clip / jnp.maximum(jnp.sqrt(squared), clip)
        factors = lax.all_to_all(
            jnp.broadcast_to(factor[None], (n_fsdp, tok)), "fsdp", 0, 0, tiled=True
        ).reshape(n_fsdp * tok)

        fresh_parts = lax.all_to_all(
            jnp.broadcast_to(fresh_noise[None], (n_dp,) + fresh_noise.shape), "dp", 0, 0, tiled=True
        )
        full_fresh = jnp.transpose(fresh_parts, (1, 0, 2)).reshape(
            fresh_noise.shape[0], n_dp * fresh_noise.shape[1]
        )

        lags = (step_value - slot_ids - 1) % BAND + 1
        columns = jnp.arange(BAND, dtype=jnp.int32)
        lag_weight = jnp.sum(
            jnp.where(columns[None, :] == lags[:, None], band_coefs[None, :], 0.0), axis=1
        )
        history_part = jnp.zeros(history.shape[1:], jnp.float32)
        for position in range(history.shape[0]):
            history_part = history_part + lag_weight[position] * history[position].astype(jnp.float32)

        full_act, full_fresh = lax.optimization_barrier((full_act, full_fresh))
        scaled = (full_act.astype(jnp.float32) * factors[:, None]).astype(jnp.bfloat16)
        gradient = lax.dot_general(
            cotangents,
            scaled,
            (((0,), (0,)), ((), ())),
            preferred_element_type=jnp.float32,
        )
        new_history = jnp.where((slot_ids == target)[:, None, None], full_fresh[None], history)
        noise_scale = noise_mult[0] * clip
        combined = lax.psum_scatter(
            gradient + noise_scale * history_part, "dp", scatter_dimension=1, tiled=True
        )
        examples = EX_DEV * n_dp * n_fsdp
        noisy_mean = (
            combined + noise_scale * band_coefs[0] * fresh_noise.astype(jnp.float32)
        ) / examples
        new_first = 0.9 * first_moment + 0.1 * noisy_mean
        new_second = 0.999 * second_moment + 0.001 * noisy_mean * noisy_mean
        step_float = step_value.astype(jnp.float32)
        corrected_first = new_first / (1.0 - jnp.power(jnp.float32(0.9), step_float))
        corrected_second = new_second / (1.0 - jnp.power(jnp.float32(0.999), step_float))
        new_weights = weights - 0.002 * corrected_first / (jnp.sqrt(corrected_second) + 1e-08)
        gathered_weights = lax.all_gather(new_weights, "dp", axis=1, tiled=True)
        return (new_weights, new_first, new_second, noisy_mean, gathered_weights, new_history)

    return body


def solution(mesh):
    n_dp = mesh.shape["dp"]
    n_fsdp = mesh.shape["fsdp"]
    in_specs = (
        P(("dp", "fsdp"), None),
        P("dp", "fsdp"),
        P(("dp", "fsdp"), None),
        P("fsdp", "dp"),
        P("fsdp", "dp"),
        P("fsdp", "dp"),
        P("fsdp", "dp"),
        P("dp", "fsdp", None),
        P("dp"),
        P(),
        P(),
        P(),
    )
    out_specs = (
        P("fsdp", "dp"),
        P("fsdp", "dp"),
        P("fsdp", "dp"),
        P("fsdp", "dp"),
        P("fsdp", None),
        P("dp", "fsdp", None),
    )
    return jax.shard_map(
        make_body(n_dp, n_fsdp),
        mesh=mesh,
        in_specs=in_specs,
        out_specs=out_specs,
        check_vma=False,
    )
```

```python
import jax
import jax.numpy as jnp
from jax import lax
from jax.sharding import PartitionSpec as P

D_IN = 4096
D_OUT = 4096
BAND = 16
GROUP_MOST = 64
EX_DEV = 8


def clip_bound():
    return ((GROUP_MOST * GROUP_MOST / 4.0 + GROUP_MOST) * D_IN * D_OUT) ** 0.5


def make_body(n_dp, n_fsdp):
    def body(
        activations,
        cotangents,
        group_ids,
        weights,
        first_moment,
        second_moment,
        fresh_noise,
        history,
        slot_ids,
        band_coefs,
        step_number,
        noise_mult,
    ):
        clip = clip_bound()
        tok = activations.shape[0]
        out_local = cotangents.shape[1]
        step_value = step_number[0]
        target = step_value % BAND

        blocks = cotangents.reshape(n_fsdp, tok, out_local)
        partial_gram = jnp.einsum("ati,asi->ats", blocks, blocks, preferred_element_type=jnp.float32)
        received = lax.all_to_all(partial_gram, "fsdp", 0, 0, tiled=True)

        gather_in, received = lax.optimization_barrier((activations, received))
        full_act = lax.all_gather(gather_in, "fsdp", axis=0, tiled=True)
        cotan_gram = received[0]
        for part in range(1, n_fsdp):
            cotan_gram = cotan_gram + received[part]
        input_gram = lax.dot_general(
            activations, activations, (((1,), (1,)), ((), ())), preferred_element_type=jnp.float32
        )
        labels = group_ids[0]
        same = labels[:, None] == labels[None, :]
        row_terms = jnp.sum(jnp.where(same, input_gram * cotan_gram, 0.0), axis=1)
        squared = jnp.sum(jnp.where(same, row_terms[None, :], 0.0), axis=1)
        factor = clip / jnp.maximum(jnp.sqrt(squared), clip)
        factors = lax.all_to_all(
            jnp.broadcast_to(factor[None], (n_fsdp, tok)), "fsdp", 0, 0, tiled=True
        ).reshape(n_fsdp * tok)

        fresh_parts = lax.all_to_all(
            jnp.broadcast_to(fresh_noise[None], (n_dp,) + fresh_noise.shape), "dp", 0, 0, tiled=True
        )
        full_fresh = jnp.transpose(fresh_parts, (1, 0, 2)).reshape(
            fresh_noise.shape[0], n_dp * fresh_noise.shape[1]
        )

        lags = (step_value - slot_ids - 1) % BAND + 1
        columns = jnp.arange(BAND, dtype=jnp.int32)
        lag_weight = jnp.sum(
            jnp.where(columns[None, :] == lags[:, None], band_coefs[None, :], 0.0), axis=1
        )
        history_part = jnp.zeros(history.shape[1:], jnp.float32)
        for position in range(history.shape[0]):
            history_part = history_part + lag_weight[position] * history[position].astype(jnp.float32)

        full_act, full_fresh = lax.optimization_barrier((full_act, full_fresh))
        scaled = (full_act.astype(jnp.float32) * factors[:, None]).astype(jnp.bfloat16)
        gradient = lax.dot_general(
            cotangents,
            scaled,
            (((0,), (0,)), ((), ())),
            preferred_element_type=jnp.float32,
        )
        new_history = jnp.where((slot_ids == target)[:, None, None], full_fresh[None], history)
        noise_scale = noise_mult[0] * clip
        combined = lax.psum_scatter(
            gradient + noise_scale * history_part, "dp", scatter_dimension=1, tiled=True
        )
        examples = EX_DEV * n_dp * n_fsdp
        noisy_mean = (
            combined + noise_scale * band_coefs[0] * fresh_noise.astype(jnp.float32)
        ) / examples
        new_first = 0.9 * first_moment + 0.1 * noisy_mean
        new_second = 0.999 * second_moment + 0.001 * noisy_mean * noisy_mean
        step_float = step_value.astype(jnp.float32)
        corrected_first = new_first / (1.0 - jnp.power(jnp.float32(0.9), step_float))
        corrected_second = new_second / (1.0 - jnp.power(jnp.float32(0.999), step_float))
        new_weights = weights - 0.002 * corrected_first / (jnp.sqrt(corrected_second) + 1e-08)
        gathered_weights = lax.all_gather(new_weights, "dp", axis=1, tiled=True)
        return (new_weights, new_first, new_second, noisy_mean, gathered_weights, new_history)

    return body


def solution(mesh):
    n_dp = mesh.shape["dp"]
    n_fsdp = mesh.shape["fsdp"]
    in_specs = (
        P(("dp", "fsdp"), None),
        P("dp", "fsdp"),
        P(("dp", "fsdp"), None),
        P("fsdp", "dp"),
        P("fsdp", "dp"),
        P("fsdp", "dp"),
        P("fsdp", "dp"),
        P("dp", "fsdp", None),
        P("dp"),
        P(),
        P(),
        P(),
    )
    out_specs = (
        P("fsdp", "dp"),
        P("fsdp", "dp"),
        P("fsdp", "dp"),
        P("fsdp", "dp"),
        P("fsdp", None),
        P("dp", "fsdp", None),
    )
    return jax.shard_map(
        make_body(n_dp, n_fsdp),
        mesh=mesh,
        in_specs=in_specs,
        out_specs=out_specs,
        check_vma=False,
    )
```

```python
import jax
import jax.numpy as jnp
from jax import lax
from jax.sharding import PartitionSpec as P

D_IN = 4096
D_OUT = 4096
BAND = 16
GROUP_MOST = 64
EX_DEV = 8


def clip_bound():
    return ((GROUP_MOST * GROUP_MOST / 4.0 + GROUP_MOST) * D_IN * D_OUT) ** 0.5


def make_body(n_dp, n_fsdp):
    def body(
        activations,
        cotangents,
        group_ids,
        weights,
        first_moment,
        second_moment,
        fresh_noise,
        history,
        slot_ids,
        band_coefs,
        step_number,
        noise_mult,
    ):
        clip = clip_bound()
        tok = activations.shape[0]
        out_local = cotangents.shape[1]
        step_value = step_number[0]
        target = step_value % BAND

        blocks = cotangents.reshape(n_fsdp, tok, out_local)
        partial_gram = jnp.einsum("ati,asi->ats", blocks, blocks, preferred_element_type=jnp.float32)
        received = lax.all_to_all(partial_gram, "fsdp", 0, 0, tiled=True)

        gather_in, received = lax.optimization_barrier((activations, received))
        full_act = lax.all_gather(gather_in, "fsdp", axis=0, tiled=True)
        cotan_gram = received[0]
        for part in range(1, n_fsdp):
            cotan_gram = cotan_gram + received[part]
        input_gram = lax.dot_general(
            activations, activations, (((1,), (1,)), ((), ())), preferred_element_type=jnp.float32
        )
        labels = group_ids[0]
        same = labels[:, None] == labels[None, :]
        row_terms = jnp.sum(jnp.where(same, input_gram * cotan_gram, 0.0), axis=1)
        squared = jnp.sum(jnp.where(same, row_terms[None, :], 0.0), axis=1)
        factor = clip / jnp.maximum(jnp.sqrt(squared), clip)
        factors = lax.all_to_all(
            jnp.broadcast_to(factor[None], (n_fsdp, tok)), "fsdp", 0, 0, tiled=True
        ).reshape(n_fsdp * tok)

        fresh_parts = lax.all_to_all(
            jnp.broadcast_to(fresh_noise[None], (n_dp,) + fresh_noise.shape), "dp", 0, 0, tiled=True
        )
        full_fresh = jnp.transpose(fresh_parts, (1, 0, 2)).reshape(
            fresh_noise.shape[0], n_dp * fresh_noise.shape[1]
        )

        lags = (step_value - slot_ids - 1) % BAND + 1
        columns = jnp.arange(BAND, dtype=jnp.int32)
        lag_weight = jnp.sum(
            jnp.where(columns[None, :] == lags[:, None], band_coefs[None, :], 0.0), axis=1
        )
        history_part = jnp.zeros(history.shape[1:], jnp.float32)
        for position in range(history.shape[0]):
            history_part = history_part + lag_weight[position] * history[position].astype(jnp.float32)

        full_act, full_fresh = lax.optimization_barrier((full_act, full_fresh))
        scaled = (full_act.astype(jnp.float32) * factors[:, None]).astype(jnp.bfloat16)
        new_history = jnp.where((slot_ids == target)[:, None, None], full_fresh[None], history)
        noise_scale = noise_mult[0] * clip

        split = out_local - out_local // 4
        d_in = scaled.shape[1]
        cols = d_in // n_dp

        def payload(lo, hi):
            grad = lax.dot_general(
                cotangents[:, lo:hi], scaled, (((0,), (0,)), ((), ())), preferred_element_type=jnp.float32
            )
            return grad + noise_scale * history_part[lo:hi]

        reduced_first = lax.psum_scatter(payload(0, split), "dp", scatter_dimension=1, tiled=True)
        second_part = jnp.transpose(
            payload(split, out_local).reshape(out_local - split, n_dp, cols), (1, 0, 2)
        )
        exchanged = lax.all_to_all(second_part, "dp", 0, 0, tiled=True)
        reduced_second = exchanged[0]
        for part in range(1, n_dp):
            reduced_second = reduced_second + exchanged[part]
        combined = jnp.concatenate([reduced_first, reduced_second], axis=0)
        examples = EX_DEV * n_dp * n_fsdp
        noisy_mean = (
            combined + noise_scale * band_coefs[0] * fresh_noise.astype(jnp.float32)
        ) / examples
        new_first = 0.9 * first_moment + 0.1 * noisy_mean
        new_second = 0.999 * second_moment + 0.001 * noisy_mean * noisy_mean
        step_float = step_value.astype(jnp.float32)
        corrected_first = new_first / (1.0 - jnp.power(jnp.float32(0.9), step_float))
        corrected_second = new_second / (1.0 - jnp.power(jnp.float32(0.999), step_float))
        new_weights = weights - 0.002 * corrected_first / (jnp.sqrt(corrected_second) + 1e-08)
        gathered_weights = lax.all_gather(new_weights, "dp", axis=1, tiled=True)
        return (new_weights, new_first, new_second, noisy_mean, gathered_weights, new_history)

    return body


def solution(mesh):
    n_dp = mesh.shape["dp"]
    n_fsdp = mesh.shape["fsdp"]
    in_specs = (
        P(("dp", "fsdp"), None),
        P("dp", "fsdp"),
        P(("dp", "fsdp"), None),
        P("fsdp", "dp"),
        P("fsdp", "dp"),
        P("fsdp", "dp"),
        P("fsdp", "dp"),
        P("dp", "fsdp", None),
        P("dp"),
        P(),
        P(),
        P(),
    )
    out_specs = (
        P("fsdp", "dp"),
        P("fsdp", "dp"),
        P("fsdp", "dp"),
        P("fsdp", "dp"),
        P("fsdp", None),
        P("dp", "fsdp", None),
    )
    return jax.shard_map(
        make_body(n_dp, n_fsdp),
        mesh=mesh,
        in_specs=in_specs,
        out_specs=out_specs,
        check_vma=False,
    )
```

```python
import jax
import jax.numpy as jnp
from jax import lax
from jax.sharding import PartitionSpec as P

D_IN = 4096
D_OUT = 4096
BAND = 16
GROUP_MOST = 64
EX_DEV = 8


def clip_bound():
    return ((GROUP_MOST * GROUP_MOST / 4.0 + GROUP_MOST) * D_IN * D_OUT) ** 0.5


def make_body(n_dp, n_fsdp):
    def body(
        activations,
        cotangents,
        group_ids,
        weights,
        first_moment,
        second_moment,
        fresh_noise,
        history,
        slot_ids,
        band_coefs,
        step_number,
        noise_mult,
    ):
        clip = clip_bound()
        tok = activations.shape[0]
        out_local = cotangents.shape[1]
        step_value = step_number[0]
        target = step_value % BAND

        blocks = cotangents.reshape(n_fsdp, tok, out_local)
        partial_gram = jnp.einsum("ati,asi->ats", blocks, blocks, preferred_element_type=jnp.float32)
        received = lax.all_to_all(partial_gram, "fsdp", 0, 0, tiled=True)

        gather_in, received = lax.optimization_barrier((activations, received))
        cotan_gram = received[0]
        for part in range(1, n_fsdp):
            cotan_gram = cotan_gram + received[part]
        input_gram = lax.dot_general(
            activations, activations, (((1,), (1,)), ((), ())), preferred_element_type=jnp.float32
        )
        labels = group_ids[0]
        same = labels[:, None] == labels[None, :]
        row_terms = jnp.sum(jnp.where(same, input_gram * cotan_gram, 0.0), axis=1)
        squared = jnp.sum(jnp.where(same, row_terms[None, :], 0.0), axis=1)
        factor = clip / jnp.maximum(jnp.sqrt(squared), clip)
        factors = lax.all_to_all(
            jnp.broadcast_to(factor[None], (n_fsdp, tok)), "fsdp", 0, 0, tiled=True
        ).reshape(n_fsdp * tok)

        full_fresh = lax.all_gather(fresh_noise, "dp", axis=1, tiled=True)

        lags = (step_value - slot_ids - 1) % BAND + 1
        columns = jnp.arange(BAND, dtype=jnp.int32)
        lag_weight = jnp.sum(
            jnp.where(columns[None, :] == lags[:, None], band_coefs[None, :], 0.0), axis=1
        )
        history_part = jnp.zeros(history.shape[1:], jnp.float32)
        for position in range(history.shape[0]):
            history_part = history_part + lag_weight[position] * history[position].astype(jnp.float32)
        noise_scale = noise_mult[0] * clip

        d_in = activations.shape[1]
        cols = d_in // n_dp
        chunks = 2
        width = cols // chunks
        act4 = gather_in.reshape(tok, n_dp, chunks, width)
        history4 = history_part.reshape(out_local, n_dp, chunks, width)
        reduced = []
        for c in range(chunks):
            own = act4[:, :, c, :]
            rows = lax.all_to_all(
                jnp.broadcast_to(own[None], (n_fsdp,) + own.shape), "fsdp", 0, 0, tiled=True
            ).reshape(n_fsdp * tok, n_dp * width)
            if c == 0:
                rows, full_fresh = lax.optimization_barrier((rows, full_fresh))
            scaled = (rows.astype(jnp.float32) * factors[:, None]).astype(jnp.bfloat16)
            grad = lax.dot_general(
                cotangents, scaled, (((0,), (0,)), ((), ())), preferred_element_type=jnp.float32
            )
            payload = grad + noise_scale * history4[:, :, c, :].reshape(out_local, n_dp * width)
            reduced.append(lax.psum_scatter(payload, "dp", scatter_dimension=1, tiled=True))
        combined = jnp.concatenate(reduced, axis=1)
        new_history = jnp.where((slot_ids == target)[:, None, None], full_fresh[None], history)
        examples = EX_DEV * n_dp * n_fsdp
        noisy_mean = (
            combined + noise_scale * band_coefs[0] * fresh_noise.astype(jnp.float32)
        ) / examples
        new_first = 0.9 * first_moment + 0.1 * noisy_mean
        new_second = 0.999 * second_moment + 0.001 * noisy_mean * noisy_mean
        step_float = step_value.astype(jnp.float32)
        corrected_first = new_first / (1.0 - jnp.power(jnp.float32(0.9), step_float))
        corrected_second = new_second / (1.0 - jnp.power(jnp.float32(0.999), step_float))
        new_weights = weights - 0.002 * corrected_first / (jnp.sqrt(corrected_second) + 1e-08)
        gathered_weights = lax.all_gather(new_weights, "dp", axis=1, tiled=True)
        return (new_weights, new_first, new_second, noisy_mean, gathered_weights, new_history)

    return body


def solution(mesh):
    n_dp = mesh.shape["dp"]
    n_fsdp = mesh.shape["fsdp"]
    in_specs = (
        P(("dp", "fsdp"), None),
        P("dp", "fsdp"),
        P(("dp", "fsdp"), None),
        P("fsdp", "dp"),
        P("fsdp", "dp"),
        P("fsdp", "dp"),
        P("fsdp", "dp"),
        P("dp", "fsdp", None),
        P("dp"),
        P(),
        P(),
        P(),
    )
    out_specs = (
        P("fsdp", "dp"),
        P("fsdp", "dp"),
        P("fsdp", "dp"),
        P("fsdp", "dp"),
        P("fsdp", None),
        P("dp", "fsdp", None),
    )
    return jax.shard_map(
        make_body(n_dp, n_fsdp),
        mesh=mesh,
        in_specs=in_specs,
        out_specs=out_specs,
        check_vma=False,
    )
```

```python
import jax
import jax.numpy as jnp
from jax import lax
from jax.sharding import PartitionSpec as P

D_IN = 4096
D_OUT = 4096
BAND = 16
GROUP_MOST = 64
EX_DEV = 8


def clip_bound():
    return ((GROUP_MOST * GROUP_MOST / 4.0 + GROUP_MOST) * D_IN * D_OUT) ** 0.5


def make_body(n_dp, n_fsdp):
    def body(
        activations,
        cotangents,
        group_ids,
        weights,
        first_moment,
        second_moment,
        fresh_noise,
        history,
        slot_ids,
        band_coefs,
        step_number,
        noise_mult,
    ):
        clip = clip_bound()
        tok = activations.shape[0]
        out_local = cotangents.shape[1]
        step_value = step_number[0]
        target = step_value % BAND

        blocks = cotangents.reshape(n_fsdp, tok, out_local)
        partial_gram = jnp.einsum("ati,asi->ats", blocks, blocks, preferred_element_type=jnp.float32)
        me = lax.axis_index("fsdp")
        cotan_gram = lax.dynamic_index_in_dim(partial_gram, me, axis=0, keepdims=False)
        for k in range(1, n_fsdp):
            to_right = lax.dynamic_index_in_dim(
                partial_gram, jnp.minimum(me + k, n_fsdp - 1), axis=0, keepdims=False
            )
            to_left = lax.dynamic_index_in_dim(
                partial_gram, jnp.maximum(me - k, 0), axis=0, keepdims=False
            )
            cotan_gram = cotan_gram + lax.ppermute(
                to_right, "fsdp", [(f, f + k) for f in range(n_fsdp - k)]
            )
            cotan_gram = cotan_gram + lax.ppermute(
                to_left, "fsdp", [(f, f - k) for f in range(k, n_fsdp)]
            )

        gather_in, cotan_gram = lax.optimization_barrier((activations, cotan_gram))
        full_act = lax.all_gather(gather_in, "fsdp", axis=0, tiled=True)
        input_gram = lax.dot_general(
            activations, activations, (((1,), (1,)), ((), ())), preferred_element_type=jnp.float32
        )
        labels = group_ids[0]
        same = labels[:, None] == labels[None, :]
        row_terms = jnp.sum(jnp.where(same, input_gram * cotan_gram, 0.0), axis=1)
        squared = jnp.sum(jnp.where(same, row_terms[None, :], 0.0), axis=1)
        factor = clip / jnp.maximum(jnp.sqrt(squared), clip)
        factors = lax.all_to_all(
            jnp.broadcast_to(factor[None], (n_fsdp, tok)), "fsdp", 0, 0, tiled=True
        ).reshape(n_fsdp * tok)

        fresh_parts = lax.all_to_all(
            jnp.broadcast_to(fresh_noise[None], (n_dp,) + fresh_noise.shape), "dp", 0, 0, tiled=True
        )
        full_fresh = jnp.transpose(fresh_parts, (1, 0, 2)).reshape(
            fresh_noise.shape[0], n_dp * fresh_noise.shape[1]
        )

        lags = (step_value - slot_ids - 1) % BAND + 1
        columns = jnp.arange(BAND, dtype=jnp.int32)
        lag_weight = jnp.sum(
            jnp.where(columns[None, :] == lags[:, None], band_coefs[None, :], 0.0), axis=1
        )
        history_part = jnp.zeros(history.shape[1:], jnp.float32)
        for position in range(history.shape[0]):
            history_part = history_part + lag_weight[position] * history[position].astype(jnp.float32)

        full_act, full_fresh = lax.optimization_barrier((full_act, full_fresh))
        scaled = (full_act.astype(jnp.float32) * factors[:, None]).astype(jnp.bfloat16)
        gradient = lax.dot_general(
            cotangents,
            scaled,
            (((0,), (0,)), ((), ())),
            preferred_element_type=jnp.float32,
        )
        new_history = jnp.where((slot_ids == target)[:, None, None], full_fresh[None], history)
        noise_scale = noise_mult[0] * clip
        combined = lax.psum_scatter(
            gradient + noise_scale * history_part, "dp", scatter_dimension=1, tiled=True
        )
        examples = EX_DEV * n_dp * n_fsdp
        noisy_mean = (
            combined + noise_scale * band_coefs[0] * fresh_noise.astype(jnp.float32)
        ) / examples
        new_first = 0.9 * first_moment + 0.1 * noisy_mean
        new_second = 0.999 * second_moment + 0.001 * noisy_mean * noisy_mean
        step_float = step_value.astype(jnp.float32)
        corrected_first = new_first / (1.0 - jnp.power(jnp.float32(0.9), step_float))
        corrected_second = new_second / (1.0 - jnp.power(jnp.float32(0.999), step_float))
        new_weights = weights - 0.002 * corrected_first / (jnp.sqrt(corrected_second) + 1e-08)
        gathered_weights = lax.all_gather(new_weights, "dp", axis=1, tiled=True)
        return (new_weights, new_first, new_second, noisy_mean, gathered_weights, new_history)

    return body


def solution(mesh):
    n_dp = mesh.shape["dp"]
    n_fsdp = mesh.shape["fsdp"]
    in_specs = (
        P(("dp", "fsdp"), None),
        P("dp", "fsdp"),
        P(("dp", "fsdp"), None),
        P("fsdp", "dp"),
        P("fsdp", "dp"),
        P("fsdp", "dp"),
        P("fsdp", "dp"),
        P("dp", "fsdp", None),
        P("dp"),
        P(),
        P(),
        P(),
    )
    out_specs = (
        P("fsdp", "dp"),
        P("fsdp", "dp"),
        P("fsdp", "dp"),
        P("fsdp", "dp"),
        P("fsdp", None),
        P("dp", "fsdp", None),
    )
    return jax.shard_map(
        make_body(n_dp, n_fsdp),
        mesh=mesh,
        in_specs=in_specs,
        out_specs=out_specs,
        check_vma=False,
    )
```

```python
import jax
import jax.numpy as jnp
from jax import lax
from jax.sharding import PartitionSpec as P
from jax.experimental.layout import Layout, with_layout_constraint

D_IN = 4096
D_OUT = 4096
BAND = 16
GROUP_MOST = 64
EX_DEV = 8


def clip_bound():
    return ((GROUP_MOST * GROUP_MOST / 4.0 + GROUP_MOST) * D_IN * D_OUT) ** 0.5


def make_body(n_dp, n_fsdp):
    def body(
        activations,
        cotangents,
        group_ids,
        weights,
        first_moment,
        second_moment,
        fresh_noise,
        history,
        slot_ids,
        band_coefs,
        step_number,
        noise_mult,
    ):
        clip = clip_bound()
        tok = activations.shape[0]
        out_local = cotangents.shape[1]
        step_value = step_number[0]
        target = step_value % BAND

        blocks = cotangents.reshape(n_fsdp, tok, out_local)
        partial_gram = jnp.einsum("ati,asi->ats", blocks, blocks, preferred_element_type=jnp.float32)
        received = lax.all_to_all(partial_gram, "fsdp", 0, 0, tiled=True)

        gather_in, received = lax.optimization_barrier((activations, received))
        full_act = lax.all_gather(gather_in, "fsdp", axis=0, tiled=True)
        cotan_gram = received[0]
        for part in range(1, n_fsdp):
            cotan_gram = cotan_gram + received[part]
        input_gram = lax.dot_general(
            activations, activations, (((1,), (1,)), ((), ())), preferred_element_type=jnp.float32
        )
        labels = group_ids[0]
        same = labels[:, None] == labels[None, :]
        row_terms = jnp.sum(jnp.where(same, input_gram * cotan_gram, 0.0), axis=1)
        squared = jnp.sum(jnp.where(same, row_terms[None, :], 0.0), axis=1)
        factor = clip / jnp.maximum(jnp.sqrt(squared), clip)
        factors = lax.all_to_all(
            jnp.broadcast_to(factor[None], (n_fsdp, tok)), "fsdp", 0, 0, tiled=True
        ).reshape(n_fsdp * tok)

        fresh_parts = lax.all_to_all(
            jnp.broadcast_to(fresh_noise[None], (n_dp,) + fresh_noise.shape), "dp", 0, 0, tiled=True
        )
        full_fresh = jnp.transpose(fresh_parts, (1, 0, 2)).reshape(
            fresh_noise.shape[0], n_dp * fresh_noise.shape[1]
        )

        lags = (step_value - slot_ids - 1) % BAND + 1
        columns = jnp.arange(BAND, dtype=jnp.int32)
        lag_weight = jnp.sum(
            jnp.where(columns[None, :] == lags[:, None], band_coefs[None, :], 0.0), axis=1
        )
        history_part = jnp.zeros(history.shape[1:], jnp.float32)
        for position in range(history.shape[0]):
            history_part = history_part + lag_weight[position] * history[position].astype(jnp.float32)

        full_act, full_fresh = lax.optimization_barrier((full_act, full_fresh))
        scaled = (full_act.astype(jnp.float32) * factors[:, None]).astype(jnp.bfloat16)
        gradient = lax.dot_general(
            cotangents,
            scaled,
            (((0,), (0,)), ((), ())),
            preferred_element_type=jnp.float32,
        )
        new_history = jnp.where((slot_ids == target)[:, None, None], full_fresh[None], history)
        noise_scale = noise_mult[0] * clip
        combined = lax.psum_scatter(
            gradient + noise_scale * history_part, "dp", scatter_dimension=1, tiled=True
        )
        examples = EX_DEV * n_dp * n_fsdp
        noisy_mean = (
            combined + noise_scale * band_coefs[0] * fresh_noise.astype(jnp.float32)
        ) / examples
        new_first = 0.9 * first_moment + 0.1 * noisy_mean
        new_second = 0.999 * second_moment + 0.001 * noisy_mean * noisy_mean
        step_float = step_value.astype(jnp.float32)
        corrected_first = new_first / (1.0 - jnp.power(jnp.float32(0.9), step_float))
        corrected_second = new_second / (1.0 - jnp.power(jnp.float32(0.999), step_float))
        new_weights = weights - 0.002 * corrected_first / (jnp.sqrt(corrected_second) + 1e-08)
        row_major = Layout(major_to_minor=(0, 1))
        gathered_weights = with_layout_constraint(
            lax.all_gather(with_layout_constraint(new_weights, row_major), "dp", axis=1, tiled=True),
            row_major,
        )
        return (new_weights, new_first, new_second, noisy_mean, gathered_weights, new_history)

    return body


def solution(mesh):
    n_dp = mesh.shape["dp"]
    n_fsdp = mesh.shape["fsdp"]
    in_specs = (
        P(("dp", "fsdp"), None),
        P("dp", "fsdp"),
        P(("dp", "fsdp"), None),
        P("fsdp", "dp"),
        P("fsdp", "dp"),
        P("fsdp", "dp"),
        P("fsdp", "dp"),
        P("dp", "fsdp", None),
        P("dp"),
        P(),
        P(),
        P(),
    )
    out_specs = (
        P("fsdp", "dp"),
        P("fsdp", "dp"),
        P("fsdp", "dp"),
        P("fsdp", "dp"),
        P("fsdp", None),
        P("dp", "fsdp", None),
    )
    return jax.shard_map(
        make_body(n_dp, n_fsdp),
        mesh=mesh,
        in_specs=in_specs,
        out_specs=out_specs,
        check_vma=False,
    )
```

```python
import jax
import jax.numpy as jnp
from jax import lax
from jax.sharding import PartitionSpec as P
from jax.experimental.layout import Layout, with_layout_constraint

D_IN = 4096
D_OUT = 4096
BAND = 16
GROUP_MOST = 64
EX_DEV = 8


def clip_bound():
    return ((GROUP_MOST * GROUP_MOST / 4.0 + GROUP_MOST) * D_IN * D_OUT) ** 0.5


def make_body(n_dp, n_fsdp):
    def body(
        activations,
        cotangents,
        group_ids,
        weights,
        first_moment,
        second_moment,
        fresh_noise,
        history,
        slot_ids,
        band_coefs,
        step_number,
        noise_mult,
    ):
        clip = clip_bound()
        tok = activations.shape[0]
        out_local = cotangents.shape[1]
        step_value = step_number[0]
        target = step_value % BAND

        blocks = cotangents.reshape(n_fsdp, tok, out_local)
        partial_gram = jnp.einsum("ati,asi->ats", blocks, blocks, preferred_element_type=jnp.float32)
        received = lax.all_to_all(partial_gram, "fsdp", 0, 0, tiled=True)

        gather_in, received = lax.optimization_barrier((activations, received))
        full_act = lax.all_gather(gather_in, "fsdp", axis=0, tiled=True)
        cotan_gram = received[0]
        for part in range(1, n_fsdp):
            cotan_gram = cotan_gram + received[part]
        input_gram = lax.dot_general(
            activations, activations, (((1,), (1,)), ((), ())), preferred_element_type=jnp.float32
        )
        labels = group_ids[0]
        same = labels[:, None] == labels[None, :]
        row_terms = jnp.sum(jnp.where(same, input_gram * cotan_gram, 0.0), axis=1)
        squared = jnp.sum(jnp.where(same, row_terms[None, :], 0.0), axis=1)
        factor = clip / jnp.maximum(jnp.sqrt(squared), clip)
        factors = lax.all_to_all(
            jnp.broadcast_to(factor[None], (n_fsdp, tok)), "fsdp", 0, 0, tiled=True
        ).reshape(n_fsdp * tok)

        fresh_parts = lax.all_to_all(
            jnp.broadcast_to(fresh_noise[None], (n_dp,) + fresh_noise.shape), "dp", 0, 0, tiled=True
        )
        full_fresh = jnp.transpose(fresh_parts, (1, 0, 2)).reshape(
            fresh_noise.shape[0], n_dp * fresh_noise.shape[1]
        )

        lags = (step_value - slot_ids - 1) % BAND + 1
        columns = jnp.arange(BAND, dtype=jnp.int32)
        lag_weight = jnp.sum(
            jnp.where(columns[None, :] == lags[:, None], band_coefs[None, :], 0.0), axis=1
        )
        history_part = jnp.zeros(history.shape[1:], jnp.float32)
        for position in range(history.shape[0]):
            history_part = history_part + lag_weight[position] * history[position].astype(jnp.float32)

        full_act, full_fresh = lax.optimization_barrier((full_act, full_fresh))
        scaled = (full_act.astype(jnp.float32) * factors[:, None]).astype(jnp.bfloat16)
        gradient = lax.dot_general(
            cotangents,
            scaled,
            (((0,), (0,)), ((), ())),
            preferred_element_type=jnp.float32,
        )
        new_history = jnp.where((slot_ids == target)[:, None, None], full_fresh[None], history)
        noise_scale = noise_mult[0] * clip
        combined = lax.psum_scatter(
            gradient + noise_scale * history_part, "dp", scatter_dimension=1, tiled=True
        )
        examples = EX_DEV * n_dp * n_fsdp
        step_float = step_value.astype(jnp.float32)
        first_scale = 1.0 - jnp.power(jnp.float32(0.9), step_float)
        second_scale = 1.0 - jnp.power(jnp.float32(0.999), step_float)

        def adam(combined_in):
            noisy = (
                combined_in + noise_scale * band_coefs[0] * fresh_noise.astype(jnp.float32)
            ) / examples
            first = 0.9 * first_moment + 0.1 * noisy
            second = 0.999 * second_moment + 0.001 * noisy * noisy
            updated = weights - 0.002 * (first / first_scale) / (jnp.sqrt(second / second_scale) + 1e-08)
            return noisy, first, second, updated

        new_weights = adam(combined)[3]
        row_major = Layout(major_to_minor=(0, 1))
        gathered_weights = with_layout_constraint(
            lax.all_gather(with_layout_constraint(new_weights, row_major), "dp", axis=1, tiled=True),
            row_major,
        )
        combined_late, new_weights = lax.optimization_barrier((combined, new_weights))
        noisy_mean, new_first, new_second, _ = adam(combined_late)
        return (new_weights, new_first, new_second, noisy_mean, gathered_weights, new_history)

    return body


def solution(mesh):
    n_dp = mesh.shape["dp"]
    n_fsdp = mesh.shape["fsdp"]
    in_specs = (
        P(("dp", "fsdp"), None),
        P("dp", "fsdp"),
        P(("dp", "fsdp"), None),
        P("fsdp", "dp"),
        P("fsdp", "dp"),
        P("fsdp", "dp"),
        P("fsdp", "dp"),
        P("dp", "fsdp", None),
        P("dp"),
        P(),
        P(),
        P(),
    )
    out_specs = (
        P("fsdp", "dp"),
        P("fsdp", "dp"),
        P("fsdp", "dp"),
        P("fsdp", "dp"),
        P("fsdp", None),
        P("dp", "fsdp", None),
    )
    return jax.shard_map(
        make_body(n_dp, n_fsdp),
        mesh=mesh,
        in_specs=in_specs,
        out_specs=out_specs,
        check_vma=False,
    )
```

```python
import jax
import jax.numpy as jnp
from jax import lax
from jax.sharding import PartitionSpec as P
from jax.experimental.layout import Layout, with_layout_constraint

D_IN = 4096
D_OUT = 4096
BAND = 16
GROUP_MOST = 64
EX_DEV = 8


def clip_bound():
    return ((GROUP_MOST * GROUP_MOST / 4.0 + GROUP_MOST) * D_IN * D_OUT) ** 0.5


def make_body(n_dp, n_fsdp):
    def body(
        activations,
        cotangents,
        group_ids,
        weights,
        first_moment,
        second_moment,
        fresh_noise,
        history,
        slot_ids,
        band_coefs,
        step_number,
        noise_mult,
    ):
        clip = clip_bound()
        tok = activations.shape[0]
        out_local = cotangents.shape[1]
        step_value = step_number[0]
        target = step_value % BAND

        blocks = cotangents.reshape(n_fsdp, tok, out_local)
        partial_gram = jnp.einsum("ati,asi->ats", blocks, blocks, preferred_element_type=jnp.float32)
        received = lax.all_to_all(partial_gram, "fsdp", 0, 0, tiled=True)

        gather_in, received = lax.optimization_barrier((activations, received))
        full_act = lax.all_gather(gather_in, "fsdp", axis=0, tiled=True)
        cotan_gram = received[0]
        for part in range(1, n_fsdp):
            cotan_gram = cotan_gram + received[part]
        input_gram = lax.dot_general(
            activations, activations, (((1,), (1,)), ((), ())), preferred_element_type=jnp.float32
        )
        labels = group_ids[0]
        same = labels[:, None] == labels[None, :]
        row_terms = jnp.sum(jnp.where(same, input_gram * cotan_gram, 0.0), axis=1)
        squared = jnp.sum(jnp.where(same, row_terms[None, :], 0.0), axis=1)
        factor = clip / jnp.maximum(jnp.sqrt(squared), clip)
        factors = lax.all_to_all(
            jnp.broadcast_to(factor[None], (n_fsdp, tok)), "fsdp", 0, 0, tiled=True
        ).reshape(n_fsdp * tok)

        fresh_parts = lax.all_to_all(
            jnp.broadcast_to(fresh_noise[None], (n_dp,) + fresh_noise.shape), "dp", 0, 0, tiled=True
        )
        full_fresh = jnp.transpose(fresh_parts, (1, 0, 2)).reshape(
            fresh_noise.shape[0], n_dp * fresh_noise.shape[1]
        )

        lags = (step_value - slot_ids - 1) % BAND + 1
        columns = jnp.arange(BAND, dtype=jnp.int32)
        lag_weight = jnp.sum(
            jnp.where(columns[None, :] == lags[:, None], band_coefs[None, :], 0.0), axis=1
        )
        history_part = jnp.zeros(history.shape[1:], jnp.float32)
        for position in range(history.shape[0]):
            history_part = history_part + lag_weight[position] * history[position].astype(jnp.float32)

        full_act, full_fresh = lax.optimization_barrier((full_act, full_fresh))
        noise_scale = noise_mult[0] * clip

        me = lax.axis_index("fsdp")
        own_cot = lax.dynamic_slice_in_dim(cotangents, me * tok, tok, axis=0)
        own_scaled = (activations.astype(jnp.float32) * factor[:, None]).astype(jnp.bfloat16)
        base = lax.dot_general(
            own_cot, own_scaled, (((0,), (0,)), ((), ())), preferred_element_type=jnp.float32
        ) + noise_scale * history_part
        base, full_fresh = lax.optimization_barrier((base, full_fresh))
        new_history = jnp.where((slot_ids == target)[:, None, None], full_fresh[None], history)
        others = [(me + j) % n_fsdp for j in range(1, n_fsdp)]
        other_rows = jnp.concatenate(
            [lax.dynamic_slice_in_dim(full_act, i * tok, tok, axis=0) for i in others], axis=0
        )
        other_factors = jnp.concatenate(
            [lax.dynamic_slice_in_dim(factors, i * tok, tok, axis=0) for i in others], axis=0
        )
        other_cot = jnp.concatenate(
            [lax.dynamic_slice_in_dim(cotangents, i * tok, tok, axis=0) for i in others], axis=0
        )
        other_scaled = (other_rows.astype(jnp.float32) * other_factors[:, None]).astype(jnp.bfloat16)
        payload = base + lax.dot_general(
            other_cot, other_scaled, (((0,), (0,)), ((), ())), preferred_element_type=jnp.float32
        )
        combined = lax.psum_scatter(payload, "dp", scatter_dimension=1, tiled=True)
        examples = EX_DEV * n_dp * n_fsdp
        step_float = step_value.astype(jnp.float32)
        first_scale = 1.0 - jnp.power(jnp.float32(0.9), step_float)
        second_scale = 1.0 - jnp.power(jnp.float32(0.999), step_float)

        def adam(combined_in):
            noisy = (
                combined_in + noise_scale * band_coefs[0] * fresh_noise.astype(jnp.float32)
            ) / examples
            first = 0.9 * first_moment + 0.1 * noisy
            second = 0.999 * second_moment + 0.001 * noisy * noisy
            updated = weights - 0.002 * (first / first_scale) / (jnp.sqrt(second / second_scale) + 1e-08)
            return noisy, first, second, updated

        new_weights = adam(combined)[3]
        row_major = Layout(major_to_minor=(0, 1))
        gathered_weights = with_layout_constraint(
            lax.all_gather(with_layout_constraint(new_weights, row_major), "dp", axis=1, tiled=True),
            row_major,
        )
        combined_late, new_weights = lax.optimization_barrier((combined, new_weights))
        noisy_mean, new_first, new_second, _ = adam(combined_late)
        return (new_weights, new_first, new_second, noisy_mean, gathered_weights, new_history)

    return body


def solution(mesh):
    n_dp = mesh.shape["dp"]
    n_fsdp = mesh.shape["fsdp"]
    in_specs = (
        P(("dp", "fsdp"), None),
        P("dp", "fsdp"),
        P(("dp", "fsdp"), None),
        P("fsdp", "dp"),
        P("fsdp", "dp"),
        P("fsdp", "dp"),
        P("fsdp", "dp"),
        P("dp", "fsdp", None),
        P("dp"),
        P(),
        P(),
        P(),
    )
    out_specs = (
        P("fsdp", "dp"),
        P("fsdp", "dp"),
        P("fsdp", "dp"),
        P("fsdp", "dp"),
        P("fsdp", None),
        P("dp", "fsdp", None),
    )
    return jax.shard_map(
        make_body(n_dp, n_fsdp),
        mesh=mesh,
        in_specs=in_specs,
        out_specs=out_specs,
        check_vma=False,
    )
```

```python
import jax
import jax.numpy as jnp
from jax import lax
from jax.sharding import PartitionSpec as P
from jax.experimental.layout import Layout, with_layout_constraint

D_IN = 4096
D_OUT = 4096
BAND = 16
GROUP_MOST = 64
EX_DEV = 8


def clip_bound():
    return ((GROUP_MOST * GROUP_MOST / 4.0 + GROUP_MOST) * D_IN * D_OUT) ** 0.5


def make_body(n_dp, n_fsdp):
    def body(
        activations,
        cotangents,
        group_ids,
        weights,
        first_moment,
        second_moment,
        fresh_noise,
        history,
        slot_ids,
        band_coefs,
        step_number,
        noise_mult,
    ):
        clip = clip_bound()
        tok = activations.shape[0]
        out_local = cotangents.shape[1]
        step_value = step_number[0]
        target = step_value % BAND

        blocks = cotangents.reshape(n_fsdp, tok, out_local)
        partial_gram = jnp.einsum("ati,asi->ats", blocks, blocks, preferred_element_type=jnp.float32)
        received = lax.all_to_all(partial_gram, "fsdp", 0, 0, tiled=True)

        gather_in, received = lax.optimization_barrier((activations, received))
        full_act = lax.all_gather(gather_in, "fsdp", axis=0, tiled=True)
        cotan_gram = received[0]
        for part in range(1, n_fsdp):
            cotan_gram = cotan_gram + received[part]
        input_gram = lax.dot_general(
            activations, activations, (((1,), (1,)), ((), ())), preferred_element_type=jnp.float32
        )
        labels = group_ids[0]
        same = labels[:, None] == labels[None, :]
        row_terms = jnp.sum(jnp.where(same, input_gram * cotan_gram, 0.0), axis=1)
        squared = jnp.sum(jnp.where(same, row_terms[None, :], 0.0), axis=1)
        factor = clip / jnp.maximum(jnp.sqrt(squared), clip)
        factors = lax.all_to_all(
            jnp.broadcast_to(factor[None], (n_fsdp, tok)), "fsdp", 0, 0, tiled=True
        ).reshape(n_fsdp * tok)

        fresh_parts = lax.all_to_all(
            jnp.broadcast_to(fresh_noise[None], (n_dp,) + fresh_noise.shape), "dp", 0, 0, tiled=True
        )
        full_fresh = jnp.transpose(fresh_parts, (1, 0, 2)).reshape(
            fresh_noise.shape[0], n_dp * fresh_noise.shape[1]
        )

        lags = (step_value - slot_ids - 1) % BAND + 1
        columns = jnp.arange(BAND, dtype=jnp.int32)
        lag_weight = jnp.sum(
            jnp.where(columns[None, :] == lags[:, None], band_coefs[None, :], 0.0), axis=1
        )
        history_part = jnp.zeros(history.shape[1:], jnp.float32)
        for position in range(history.shape[0]):
            history_part = history_part + lag_weight[position] * history[position].astype(jnp.float32)

        full_act, full_fresh = lax.optimization_barrier((full_act, full_fresh))
        noise_scale = noise_mult[0] * clip

        me = lax.axis_index("fsdp")
        own_cot = lax.dynamic_slice_in_dim(cotangents, me * tok, tok, axis=0)
        own_scaled = (activations.astype(jnp.float32) * factor[:, None]).astype(jnp.bfloat16)
        base = lax.dot_general(
            own_cot, own_scaled, (((0,), (0,)), ((), ())), preferred_element_type=jnp.float32
        ) + noise_scale * history_part
        base, full_fresh = lax.optimization_barrier((base, full_fresh))
        new_history = jnp.where((slot_ids == target)[:, None, None], full_fresh[None], history)
        row_block = jnp.arange(cotangents.shape[0], dtype=jnp.int32) // tok
        other_cot = jnp.where((row_block == me)[:, None], jnp.zeros_like(cotangents), cotangents)
        other_scaled = (full_act.astype(jnp.float32) * factors[:, None]).astype(jnp.bfloat16)
        payload = base + lax.dot_general(
            other_cot, other_scaled, (((0,), (0,)), ((), ())), preferred_element_type=jnp.float32
        )
        combined = lax.psum_scatter(payload, "dp", scatter_dimension=1, tiled=True)
        examples = EX_DEV * n_dp * n_fsdp
        step_float = step_value.astype(jnp.float32)
        first_scale = 1.0 - jnp.power(jnp.float32(0.9), step_float)
        second_scale = 1.0 - jnp.power(jnp.float32(0.999), step_float)

        def adam(combined_in):
            noisy = (
                combined_in + noise_scale * band_coefs[0] * fresh_noise.astype(jnp.float32)
            ) / examples
            first = 0.9 * first_moment + 0.1 * noisy
            second = 0.999 * second_moment + 0.001 * noisy * noisy
            updated = weights - 0.002 * (first / first_scale) / (jnp.sqrt(second / second_scale) + 1e-08)
            return noisy, first, second, updated

        new_weights = adam(combined)[3]
        row_major = Layout(major_to_minor=(0, 1))
        gathered_weights = with_layout_constraint(
            lax.all_gather(with_layout_constraint(new_weights, row_major), "dp", axis=1, tiled=True),
            row_major,
        )
        combined_late, new_weights = lax.optimization_barrier((combined, new_weights))
        noisy_mean, new_first, new_second, _ = adam(combined_late)
        return (new_weights, new_first, new_second, noisy_mean, gathered_weights, new_history)

    return body


def solution(mesh):
    n_dp = mesh.shape["dp"]
    n_fsdp = mesh.shape["fsdp"]
    in_specs = (
        P(("dp", "fsdp"), None),
        P("dp", "fsdp"),
        P(("dp", "fsdp"), None),
        P("fsdp", "dp"),
        P("fsdp", "dp"),
        P("fsdp", "dp"),
        P("fsdp", "dp"),
        P("dp", "fsdp", None),
        P("dp"),
        P(),
        P(),
        P(),
    )
    out_specs = (
        P("fsdp", "dp"),
        P("fsdp", "dp"),
        P("fsdp", "dp"),
        P("fsdp", "dp"),
        P("fsdp", None),
        P("dp", "fsdp", None),
    )
    return jax.shard_map(
        make_body(n_dp, n_fsdp),
        mesh=mesh,
        in_specs=in_specs,
        out_specs=out_specs,
        check_vma=False,
    )
```
